1024 devices in a mesh: seq: 64 (over z_lo, y), head: 8 (over z_hi, x), fsdp: 2 (over core).
Axes of the slice: x: 4, y: 8, z: 16 (z_hi: 2, z_lo: 8; z = z_hi * 8 + z_lo), core: 2. Of those that a mesh axis runs over, the one named last changes fastest.
Arguments:
- query: bfloat16 [2, 8192, 2048], P('fsdp', 'seq', 'head'), may hold values from -6 to 6
- keys: bfloat16 [2, 8192, 2048], P('fsdp', 'seq', 'head'), may hold values from -6 to 6
- values: bfloat16 [2, 8192, 2048], P('fsdp', 'seq', 'head'), may hold values from -6 to 6
- grad_out: bfloat16 [2, 8192, 4096], P('fsdp', 'seq'), may hold values from -16 to 16
- w_out: bfloat16 [2048, 4096], P('head', 'fsdp'), may hold values from -0.125 to 0.125
- link_flags: int32 [64, 6], P('seq'), may hold values 0 or 1
Outputs:
- grad_query: bfloat16 [2, 8192, 2048], P('fsdp', 'seq', 'head')
- grad_keys: bfloat16 [2, 8192, 2048], P('fsdp', 'seq', 'head')
- grad_values: bfloat16 [2, 8192, 2048], P('fsdp', 'seq', 'head')
- grad_w_out_t: float32 [4096, 2048], P('seq', ('head', 'fsdp'))
The draws below stay inside these ranges and needn't reach their ends.
All inputs are finite; a program needn't handle non-finite values. No bound on the sum of `link_flags` on one device may be relied on, other than what follows from the above.
Results may differ from the reference program's by a relative error of at most 0.01.
Values may be sent and summed in bfloat16 or wider, within the bound.
No kernel may reach another device: no remote copies, remote signals or barrier semaphores. Data moves between devices by JAX's collectives and lax.ppermute only.
A program may use at most 32 MiB of HBM per device.

```python
import math
import jax
import jax.numpy as jnp
from jax import lax

D = 4096
HD = 128
BLK = 128
HEADS = 16
SEQ_BITS = 6
SEQLEN = 8192
BATCH = 2
N_SEQ = 64


def query_key_pair(key):
    query_key = jax.random.fold_in(key, 11)
    keys_key = jax.random.fold_in(key, 12)
    shape = (BATCH, SEQLEN, HEADS * HD)
    queries = jnp.clip(jax.random.normal(query_key, shape, jnp.float32), -6.0, 6.0)
    keyset = jnp.clip(jax.random.normal(keys_key, shape, jnp.float32), -6.0, 6.0)
    return (queries.astype(jnp.bfloat16), keyset.astype(jnp.bfloat16))


def draw_query(key, part):
    return query_key_pair(key)[0]


def draw_keys(key, part):
    return query_key_pair(key)[1]


def touch_ends(values, stream_key, low, largest):
    shape = values.shape
    index_at = [jax.random.randint(jax.random.fold_in(stream_key, axis), (), 0, shape[axis]) for axis in range(len(shape))]
    values = values.at[tuple(index_at)].set(low)
    longest = shape.index(max(shape))
    index_at[longest] = (index_at[longest] + 1) % shape[longest]
    return values.at[tuple(index_at)].set(largest)


def raised(entries, own_key, source, target, parts, factor):
    def block_of(axis_at):
        return (jnp.arange(entries.shape[axis_at]) // (entries.shape[axis_at] // parts)).reshape((-1,) + (1,) * (entries.ndim - 1 - axis_at))

    first = jax.random.permutation(own_key, parts)[block_of(target)]
    far = (block_of(target) + parts // 2) % parts
    return jnp.where((block_of(source) == first) | (block_of(source) == far), factor * entries, entries)


def steps_of(key, dims, split, smallest, high):
    def one(position, parts):
        draws = jax.random.uniform(jax.random.fold_in(jax.random.fold_in(key, 6), position), (parts,), jnp.float32, smallest / len(split), high / len(split))
        return jnp.repeat(jnp.exp(draws), dims[position] // parts).reshape((-1,) + (1,) * (len(dims) - position - 1))

    loudness = one(*split[0])
    for cut in split[1:]:
        loudness = loudness * one(*cut)
    return loudness


def scatter_about(own_key, shape, spread, reach, pieces=(), kind=jnp.bfloat16):
    result = jax.random.normal(own_key, shape, jnp.float32) * spread
    if len(pieces) > 0:
        result = steps_of(own_key, shape, pieces, -0.22, 0.18) * result
    return jnp.clip(result, min=-reach, max=reach).astype(kind)


def heavy_noise(own_key, extent, spread, most, split, heavy, held_as=jnp.bfloat16):
    values = spread * jax.random.normal(own_key, extent, jnp.float32)
    if split:
        values = values * steps_of(own_key, extent, split, -0.22, 0.18)
    return jnp.clip(raised(values, jax.random.fold_in(own_key, 3), *heavy), -most, most).astype(held_as)


def setup_inputs(seed: int = 0) -> dict:
    key_of = jax.random.split(jax.random.key(seed), 7)
    return {
        "query": draw_query(jax.random.fold_in(key_of[6], 71), 0),
        "keys": draw_keys(jax.random.fold_in(key_of[6], 71), 0),
        "values": scatter_about(key_of[2], (BATCH, SEQLEN, HEADS * HD), 1.0, 6.0, ((0, 2), (1, 64), (2, 8))),
        "grad_out": heavy_noise(key_of[3], (BATCH, SEQLEN, D), 1.0, 16.0, ((0, 2), (1, 64)), (1, 2, 64, 4.0)),
        "w_out": scatter_about(key_of[4], (HEADS * HD, D), (HEADS * HD) ** -0.5, 0.125, ((0, 8), (1, 2))),
        "link_flags": touch_ends((jax.random.randint(key_of[5], (N_SEQ, SEQ_BITS), 0, 4) < 3).astype(jnp.int32), jax.random.fold_in(key_of[5], 1), 0, 1),
    }


def split_heads(array, nblocks):
    shaped = array.reshape(BATCH, nblocks, BLK, HEADS, HD).transpose(0, 3, 1, 2, 4)
    return shaped.reshape(BATCH * HEADS, nblocks, BLK, HD)

def merge_heads(array, nblocks):
    shaped = array.reshape(BATCH, HEADS, nblocks, BLK, HD).transpose(0, 2, 3, 1, 4)
    return shaped.reshape(BATCH, nblocks * BLK, HEADS * HD)

def reference(query, keys, values, grad_out, w_out, link_flags):
    score_scale = 1.0 / math.sqrt(HD)
    nblocks = N_SEQ
    levels = SEQ_BITS
    base = jnp.arange(nblocks, dtype=jnp.int32)
    partner = jnp.stack([base] + [jnp.bitwise_xor(base, 2 ** level).astype(jnp.int32) for level in range(levels)], axis=1)
    spots = jnp.arange(BLK, dtype=jnp.int32)
    causal = spots[None, :] <= spots[:, None]
    link_on = jnp.concatenate([jnp.ones((nblocks, 1), dtype=bool), link_flags > 0], axis=1)
    first_slot = jnp.arange(levels + 1, dtype=jnp.int32) == 0
    allowed = jnp.where(first_slot[None, None, :, None], causal[None, :, None, :], link_on[:, None, :, None])
    grad_rows = grad_out.reshape(BATCH * SEQLEN, D)
    grad_att = jnp.dot(grad_rows, w_out.T, preferred_element_type=jnp.float32).astype(jnp.bfloat16)
    stacked = (split_heads(query, nblocks), split_heads(keys, nblocks), split_heads(values, nblocks), split_heads(grad_att.reshape(BATCH, SEQLEN, HEADS * HD), nblocks))

    def one_head(operands):
        query_blocks, key_blocks, value_blocks, grad_blocks = operands
        query_wide = query_blocks.astype(jnp.float32)
        grad_wide = grad_blocks.astype(jnp.float32)
        key_near = key_blocks[partner].astype(jnp.float32)
        value_near = value_blocks[partner].astype(jnp.float32)
        scores = jnp.einsum('itc,imuc->itmu', query_wide, key_near) * score_scale
        scores = jnp.where(allowed, scores, -jnp.inf)
        row_max = lax.optimization_barrier(jnp.max(scores, axis=(2, 3), keepdims=True))
        raw = jnp.exp(scores - row_max)
        softmax = raw / lax.optimization_barrier(jnp.sum(raw, axis=(2, 3), keepdims=True))
        probs_low = softmax.astype(jnp.bfloat16)
        attended = jnp.einsum('itmu,imuc->itc', probs_low.astype(jnp.float32), value_near).astype(jnp.bfloat16)
        grad_probs = jnp.einsum('itc,imuc->itmu', grad_wide, value_near)
        row_dot = lax.optimization_barrier(jnp.sum(softmax * grad_probs, axis=(2, 3), keepdims=True))
        grad_scores = (softmax * (grad_probs - row_dot) * score_scale).astype(jnp.bfloat16)
        grad_query = jnp.einsum('itmu,imuc->itc', grad_scores.astype(jnp.float32), key_near).astype(jnp.bfloat16)
        key_terms = jnp.einsum('itmu,itc->imuc', grad_scores.astype(jnp.float32), query_wide)
        value_terms = jnp.einsum('itmu,itc->imuc', probs_low.astype(jnp.float32), grad_wide)
        grad_key = key_terms[:, 0]
        grad_value = value_terms[:, 0]
        for level in range(levels):
            key_low = lax.optimization_barrier(key_terms[:, level + 1].astype(jnp.bfloat16)).astype(jnp.float32)
            value_low = lax.optimization_barrier(value_terms[:, level + 1].astype(jnp.bfloat16)).astype(jnp.float32)
            grad_key = grad_key + key_low[partner[:, level + 1]]
            grad_value = grad_value + value_low[partner[:, level + 1]]
        return (attended, grad_query, grad_key.astype(jnp.bfloat16), grad_value.astype(jnp.bfloat16))
    results = lax.map(one_head, stacked)
    attended = merge_heads(results[0], nblocks)
    grad_w = jnp.dot(grad_rows.T, attended.reshape(BATCH * SEQLEN, HEADS * HD), preferred_element_type=jnp.float32)
    return (merge_heads(results[1], nblocks), merge_heads(results[2], nblocks), merge_heads(results[3], nblocks), grad_w)
```

```python
import math

import jax
import jax.numpy as jnp
from jax import lax
from jax.sharding import PartitionSpec as P

D = 4096
HD = 128


def swapped(shard, axis, distance):
    return lax.ppermute(shard, axis, [(i, i ^ 1 << distance) for i in range(lax.axis_size(axis))])


def halving_scatter(partial, axis, levels):
    rows, cols = partial.shape
    here = lax.axis_index(axis)
    block = rows >> levels
    pieces = partial.reshape((2,) * levels + (2, block // 2, cols))
    low = [b for b in range(levels) if b < (levels + 1) // 2]
    high = [b for b in range(levels) if b >= (levels + 1) // 2]
    first = [b for pair in zip(low, high) for b in pair] + low[len(high):]
    second = [b for pair in zip(high, low) for b in pair] + low[len(high):]
    halves = [pieces[..., 0, :, :], pieces[..., 1, :, :]]
    bits_left = [list(range(levels - 1, -1, -1)), list(range(levels - 1, -1, -1))]
    for step in range(levels):
        for h, order in enumerate((first, second)):
            bit = order[step]
            at = bits_left[h].index(bit)
            mine = (here >> bit) & 1
            keep = lax.dynamic_index_in_dim(halves[h], mine, at, keepdims=False)
            send = lax.dynamic_index_in_dim(halves[h], 1 - mine, at, keepdims=False)
            halves[h] = keep + swapped(send, axis, bit)
            bits_left[h].pop(at)
    return jnp.concatenate(halves, axis=0)


def per_device(query, keys, values, grad_out, w_out, link_flags):
    local_seqs, block_len, local_width = query.shape
    local_heads = local_width // HD
    levels = lax.axis_size("seq").bit_length() - 1
    score_scale = 1.0 / math.sqrt(HD)
    key_value = jnp.stack([keys, values])
    collected = [key_value]
    for level in range(levels):
        collected.append(swapped(key_value, "seq", level))
    slots = levels + 1
    near_all = jnp.stack(collected).reshape(slots, 2, local_seqs, block_len, local_heads, HD)
    key_near = near_all[:, 0]
    value_near = near_all[:, 1]
    query_heads = query.reshape(local_seqs, block_len, local_heads, HD)
    spots = jnp.arange(block_len, dtype=jnp.int32)
    causal = spots[None, :] <= spots[:, None]
    link_on = jnp.concatenate([jnp.ones((1,), dtype=bool), link_flags[0] > 0])
    first_slot = jnp.arange(slots, dtype=jnp.int32) == 0
    allowed = jnp.where(first_slot[None, :, None], causal[:, None, :], link_on[None, :, None])
    scores = (
        jnp.einsum("sthc,msuhc->shtmu", query_heads, key_near, preferred_element_type=jnp.float32)
        * score_scale
    )
    scores = jnp.where(allowed[None, None], scores, -jnp.inf)
    row_max = jnp.max(scores, axis=(3, 4), keepdims=True)
    raw = jnp.exp(scores - row_max)
    softmax = raw / jnp.sum(raw, axis=(3, 4), keepdims=True)
    probs_low = softmax.astype(jnp.bfloat16)
    attended = jnp.einsum(
        "shtmu,msuhc->sthc", probs_low, value_near, preferred_element_type=jnp.float32
    ).astype(jnp.bfloat16)
    grad_rows = grad_out.reshape(local_seqs * block_len, D)
    grad_rows_other = swapped(grad_rows, "fsdp", 0)
    columns = grad_rows
    grad_att = lax.dot_general(
        columns,
        lax.all_gather(w_out, "fsdp", axis=1, tiled=True),
        (((1,), (1,)), ((), ())),
        preferred_element_type=jnp.float32,
    ).astype(jnp.bfloat16)
    grad_heads = grad_att.reshape(local_seqs, block_len, local_heads, HD)
    attended_rows = attended.reshape(local_seqs * block_len, local_width)
    fsdp_size = lax.axis_size("fsdp")
    fsdp_at = lax.axis_index("fsdp")
    share = local_width // fsdp_size
    own_cols = lax.dynamic_slice_in_dim(attended_rows, fsdp_at * share, share, axis=1)
    given_cols = lax.dynamic_slice_in_dim(attended_rows, (1 - fsdp_at) * share, share, axis=1)
    taken_cols = swapped(given_cols, "fsdp", 0)
    token_rows = jnp.concatenate([grad_rows, grad_rows_other], axis=0)
    token_cols = jnp.concatenate([own_cols, taken_cols], axis=0)
    partial = lax.dot_general(
        token_rows, token_cols, (((0,), (0,)), ((), ())), preferred_element_type=jnp.float32
    )
    grad_w = halving_scatter(partial, "seq", levels)
    grad_probs = jnp.einsum(
        "sthc,msuhc->shtmu", grad_heads, value_near, preferred_element_type=jnp.float32
    )
    row_dot = jnp.sum(softmax * grad_probs, axis=(3, 4), keepdims=True)
    grad_scores = (softmax * (grad_probs - row_dot) * score_scale).astype(jnp.bfloat16)
    grad_query = jnp.einsum(
        "shtmu,msuhc->sthc", grad_scores, key_near, preferred_element_type=jnp.float32
    ).astype(jnp.bfloat16)
    key_terms = jnp.einsum(
        "shtmu,sthc->msuhc", grad_scores, query_heads, preferred_element_type=jnp.float32
    )
    value_terms = jnp.einsum(
        "shtmu,sthc->msuhc", probs_low, grad_heads, preferred_element_type=jnp.float32
    )
    grad_key = key_terms[0]
    grad_value = value_terms[0]
    for level in range(levels):
        outgoing = jnp.stack([key_terms[level + 1], value_terms[level + 1]]).astype(jnp.bfloat16)
        returned = swapped(outgoing, "seq", level)
        grad_key = grad_key + returned[0].astype(jnp.float32)
        grad_value = grad_value + returned[1].astype(jnp.float32)
    shape_out = (local_seqs, block_len, local_width)
    return (
        grad_query.reshape(shape_out),
        grad_key.astype(jnp.bfloat16).reshape(shape_out),
        grad_value.astype(jnp.bfloat16).reshape(shape_out),
        grad_w,
    )


def solution(mesh):
    in_specs = (
        P("fsdp", "seq", "head"),
        P("fsdp", "seq", "head"),
        P("fsdp", "seq", "head"),
        P("fsdp", "seq", None),
        P("head", "fsdp"),
        P("seq", None),
    )
    out_specs = (
        P("fsdp", "seq", "head"),
        P("fsdp", "seq", "head"),
        P("fsdp", "seq", "head"),
        P("seq", ("head", "fsdp")),
    )
    return jax.shard_map(
        per_device, mesh=mesh, in_specs=in_specs, out_specs=out_specs, check_vma=False
    )
```

```python
import math

import jax
import jax.numpy as jnp
from jax import lax
from jax.sharding import PartitionSpec as P

D = 4096
HD = 128


def swapped(shard, axis, distance):
    return lax.ppermute(shard, axis, [(i, i ^ 1 << distance) for i in range(lax.axis_size(axis))])


def per_device(query, keys, values, grad_out, w_out, link_flags):
    local_seqs, block_len, local_width = query.shape
    local_heads = local_width // HD
    levels = lax.axis_size("seq").bit_length() - 1
    score_scale = 1.0 / math.sqrt(HD)
    key_value = jnp.stack([keys, values])
    collected = [key_value]
    for level in range(levels):
        collected.append(swapped(key_value, "seq", level))
    slots = levels + 1
    near_all = jnp.stack(collected).reshape(slots, 2, local_seqs, block_len, local_heads, HD)
    key_near = near_all[:, 0]
    value_near = near_all[:, 1]
    query_heads = query.reshape(local_seqs, block_len, local_heads, HD)
    spots = jnp.arange(block_len, dtype=jnp.int32)
    causal = spots[None, :] <= spots[:, None]
    link_on = jnp.concatenate([jnp.ones((1,), dtype=bool), link_flags[0] > 0])
    first_slot = jnp.arange(slots, dtype=jnp.int32) == 0
    allowed = jnp.where(first_slot[None, :, None], causal[:, None, :], link_on[None, :, None])
    scores = (
        jnp.einsum("sthc,msuhc->shtmu", query_heads, key_near, preferred_element_type=jnp.float32)
        * score_scale
    )
    scores = jnp.where(allowed[None, None], scores, -jnp.inf)
    row_max = jnp.max(scores, axis=(3, 4), keepdims=True)
    raw = jnp.exp(scores - row_max)
    softmax = raw / jnp.sum(raw, axis=(3, 4), keepdims=True)
    probs_low = softmax.astype(jnp.bfloat16)
    attended = jnp.einsum(
        "shtmu,msuhc->sthc", probs_low, value_near, preferred_element_type=jnp.float32
    ).astype(jnp.bfloat16)
    grad_rows = grad_out.reshape(local_seqs * block_len, D)
    grad_rows_other = swapped(grad_rows, "fsdp", 0)
    columns = grad_rows
    grad_att = lax.dot_general(
        columns,
        lax.all_gather(w_out, "fsdp", axis=1, tiled=True),
        (((1,), (1,)), ((), ())),
        preferred_element_type=jnp.float32,
    ).astype(jnp.bfloat16)
    grad_heads = grad_att.reshape(local_seqs, block_len, local_heads, HD)
    attended_rows = attended.reshape(local_seqs * block_len, local_width)
    fsdp_size = lax.axis_size("fsdp")
    fsdp_at = lax.axis_index("fsdp")
    share = local_width // fsdp_size
    own_cols = lax.dynamic_slice_in_dim(attended_rows, fsdp_at * share, share, axis=1)
    given_cols = lax.dynamic_slice_in_dim(attended_rows, (1 - fsdp_at) * share, share, axis=1)
    taken_cols = swapped(given_cols, "fsdp", 0)
    token_rows = jnp.concatenate([grad_rows, grad_rows_other], axis=0)
    token_cols = jnp.concatenate([own_cols, taken_cols], axis=0)
    partial = lax.dot_general(
        token_rows, token_cols, (((0,), (0,)), ((), ())), preferred_element_type=jnp.float32
    )
    n_seq = lax.axis_size("seq")
    pieces = partial.reshape(n_seq, partial.shape[0] // n_seq, partial.shape[1])
    grad_w = jnp.sum(lax.all_to_all(pieces.astype(jnp.bfloat16), "seq", 0, 0, tiled=False).astype(jnp.float32), axis=0)
    grad_probs = jnp.einsum(
        "sthc,msuhc->shtmu", grad_heads, value_near, preferred_element_type=jnp.float32
    )
    row_dot = jnp.sum(softmax * grad_probs, axis=(3, 4), keepdims=True)
    grad_scores = (softmax * (grad_probs - row_dot) * score_scale).astype(jnp.bfloat16)
    grad_query = jnp.einsum(
        "shtmu,msuhc->sthc", grad_scores, key_near, preferred_element_type=jnp.float32
    ).astype(jnp.bfloat16)
    key_terms = jnp.einsum(
        "shtmu,sthc->msuhc", grad_scores, query_heads, preferred_element_type=jnp.float32
    )
    value_terms = jnp.einsum(
        "shtmu,sthc->msuhc", probs_low, grad_heads, preferred_element_type=jnp.float32
    )
    grad_key = key_terms[0]
    grad_value = value_terms[0]
    for level in range(levels):
        outgoing = jnp.stack([key_terms[level + 1], value_terms[level + 1]]).astype(jnp.bfloat16)
        returned = swapped(outgoing, "seq", level)
        grad_key = grad_key + returned[0].astype(jnp.float32)
        grad_value = grad_value + returned[1].astype(jnp.float32)
    shape_out = (local_seqs, block_len, local_width)
    return (
        grad_query.reshape(shape_out),
        grad_key.astype(jnp.bfloat16).reshape(shape_out),
        grad_value.astype(jnp.bfloat16).reshape(shape_out),
        grad_w,
    )


def solution(mesh):
    in_specs = (
        P("fsdp", "seq", "head"),
        P("fsdp", "seq", "head"),
        P("fsdp", "seq", "head"),
        P("fsdp", "seq", None),
        P("head", "fsdp"),
        P("seq", None),
    )
    out_specs = (
        P("fsdp", "seq", "head"),
        P("fsdp", "seq", "head"),
        P("fsdp", "seq", "head"),
        P("seq", ("head", "fsdp")),
    )
    return jax.shard_map(
        per_device, mesh=mesh, in_specs=in_specs, out_specs=out_specs, check_vma=False
    )
```

```python
import math

import jax
import jax.numpy as jnp
from jax import lax
from jax.sharding import PartitionSpec as P


D = 4096
HD = 128


SEQ = ("seq_hi", "seq_lo")


def size_of(axis):
    names = axis if isinstance(axis, tuple) else (axis,)
    return math.prod(lax.axis_size(name) for name in names)


def swapped(shard, axis, distance):
    return lax.ppermute(shard, axis, [(i, i ^ 1 << distance) for i in range(size_of(axis))])


def per_device_body(query, keys, values, grad_out, w_out, link_flags):
    local_seqs, block_len, local_width = query.shape
    local_heads = local_width // HD
    levels = size_of(SEQ).bit_length() - 1
    score_scale = 1.0 / math.sqrt(HD)
    key_value = jnp.stack([keys, values])
    collected = [key_value]
    for level in range(levels):
        collected.append(swapped(key_value, SEQ, level))
    slots = levels + 1
    near_all = jnp.stack(collected).reshape(slots, 2, local_seqs, block_len, local_heads, HD)
    key_near = near_all[:, 0]
    value_near = near_all[:, 1]
    query_heads = query.reshape(local_seqs, block_len, local_heads, HD)
    spots = jnp.arange(block_len, dtype=jnp.int32)
    causal = spots[None, :] <= spots[:, None]
    link_on = jnp.concatenate([jnp.ones((1,), dtype=bool), link_flags[0] > 0])
    first_slot = jnp.arange(slots, dtype=jnp.int32) == 0
    allowed = jnp.where(first_slot[None, :, None], causal[:, None, :], link_on[None, :, None])
    scores = (
        jnp.einsum("sthc,msuhc->shtmu", query_heads, key_near, preferred_element_type=jnp.float32)
        * score_scale
    )
    scores = jnp.where(allowed[None, None], scores, -jnp.inf)
    row_max = jnp.max(scores, axis=(3, 4), keepdims=True)
    raw = jnp.exp(scores - row_max)
    softmax = raw / jnp.sum(raw, axis=(3, 4), keepdims=True)
    probs_low = softmax.astype(jnp.bfloat16)
    attended = jnp.einsum(
        "shtmu,msuhc->sthc", probs_low, value_near, preferred_element_type=jnp.float32
    ).astype(jnp.bfloat16)
    grad_rows = grad_out.reshape(local_seqs * block_len, D)
    grad_rows_other = swapped(grad_rows, "fsdp", 0)
    columns = grad_rows
    grad_att = lax.dot_general(
        columns,
        lax.all_gather(w_out, "fsdp", axis=1, tiled=True),
        (((1,), (1,)), ((), ())),
        preferred_element_type=jnp.float32,
    ).astype(jnp.bfloat16)
    grad_heads = grad_att.reshape(local_seqs, block_len, local_heads, HD)
    attended_rows = attended.reshape(local_seqs * block_len, local_width)
    fsdp_size = lax.axis_size("fsdp")
    fsdp_at = lax.axis_index("fsdp")
    share = local_width // fsdp_size
    own_cols = lax.dynamic_slice_in_dim(attended_rows, fsdp_at * share, share, axis=1)
    given_cols = lax.dynamic_slice_in_dim(attended_rows, (1 - fsdp_at) * share, share, axis=1)
    taken_cols = swapped(given_cols, "fsdp", 0)
    token_rows = jnp.concatenate([grad_rows, grad_rows_other], axis=0)
    token_cols = jnp.concatenate([own_cols, taken_cols], axis=0)
    partial = lax.dot_general(
        token_rows, token_cols, (((0,), (0,)), ((), ())), preferred_element_type=jnp.float32
    )
    n_hi = lax.axis_size("seq_hi")
    n_lo = lax.axis_size("seq_lo")
    pieces = partial.reshape(n_hi, n_lo, partial.shape[0] // (n_hi * n_lo), partial.shape[1])
    inner = lax.all_to_all(pieces.astype(jnp.bfloat16), "seq_lo", 1, 1, tiled=False)
    inner = jnp.sum(inner.astype(jnp.float32), axis=1)
    outer = lax.all_to_all(inner.astype(jnp.bfloat16), "seq_hi", 0, 0, tiled=False)
    grad_w = jnp.sum(outer.astype(jnp.float32), axis=0)
    grad_probs = jnp.einsum(
        "sthc,msuhc->shtmu", grad_heads, value_near, preferred_element_type=jnp.float32
    )
    row_dot = jnp.sum(softmax * grad_probs, axis=(3, 4), keepdims=True)
    grad_scores = (softmax * (grad_probs - row_dot) * score_scale).astype(jnp.bfloat16)
    grad_query = jnp.einsum(
        "shtmu,msuhc->sthc", grad_scores, key_near, preferred_element_type=jnp.float32
    ).astype(jnp.bfloat16)
    key_terms = jnp.einsum(
        "shtmu,sthc->msuhc", grad_scores, query_heads, preferred_element_type=jnp.float32
    )
    value_terms = jnp.einsum(
        "shtmu,sthc->msuhc", probs_low, grad_heads, preferred_element_type=jnp.float32
    )
    grad_key = key_terms[0]
    grad_value = value_terms[0]
    for level in range(levels):
        outgoing = jnp.stack([key_terms[level + 1], value_terms[level + 1]]).astype(jnp.bfloat16)
        returned = swapped(outgoing, SEQ, level)
        grad_key = grad_key + returned[0].astype(jnp.float32)
        grad_value = grad_value + returned[1].astype(jnp.float32)
    shape_out = (local_seqs, block_len, local_width)
    return (
        grad_query.reshape(shape_out),
        grad_key.astype(jnp.bfloat16).reshape(shape_out),
        grad_value.astype(jnp.bfloat16).reshape(shape_out),
        grad_w,
    )


def solution(mesh):
    n_seq = mesh.shape["seq"]
    n_lo = min(8, n_seq)
    devices = mesh.devices.reshape(n_seq // n_lo, n_lo, *mesh.devices.shape[1:])
    mesh = jax.sharding.Mesh(devices, SEQ + mesh.axis_names[1:])
    in_specs = (
        P("fsdp", SEQ, "head"),
        P("fsdp", SEQ, "head"),
        P("fsdp", SEQ, "head"),
        P("fsdp", SEQ, None),
        P("head", "fsdp"),
        P(SEQ, None),
    )
    out_specs = (
        P("fsdp", SEQ, "head"),
        P("fsdp", SEQ, "head"),
        P("fsdp", SEQ, "head"),
        P(SEQ, ("head", "fsdp")),
    )
    return jax.shard_map(
        per_device_body, mesh=mesh, in_specs=in_specs, out_specs=out_specs, check_vma=False
    )
```

```python
import math

import jax
import jax.numpy as jnp
from jax import lax
from jax.sharding import PartitionSpec as P


D = 4096
HD = 128


SEQ = ("seq_hi", "seq_lo")


def size_of(axis):
    names = axis if isinstance(axis, tuple) else (axis,)
    return math.prod(lax.axis_size(name) for name in names)


def swapped(shard, axis, distance):
    return lax.ppermute(shard, axis, [(i, i ^ 1 << distance) for i in range(size_of(axis))])


def per_device_body(query, keys, values, grad_out, w_out, link_flags):
    local_seqs, block_len, local_width = query.shape
    local_heads = local_width // HD
    levels = size_of(SEQ).bit_length() - 1
    score_scale = 1.0 / math.sqrt(HD)
    key_value = jnp.stack([keys, values])
    collected = [key_value]
    for level in range(levels):
        collected.append(swapped(key_value, SEQ, level))
    slots = levels + 1
    near_all = jnp.stack(collected).reshape(slots, 2, local_seqs, block_len, local_heads, HD)
    key_near = near_all[:, 0]
    value_near = near_all[:, 1]
    query_heads = query.reshape(local_seqs, block_len, local_heads, HD)
    spots = jnp.arange(block_len, dtype=jnp.int32)
    causal = spots[None, :] <= spots[:, None]
    link_on = jnp.concatenate([jnp.ones((1,), dtype=bool), link_flags[0] > 0])
    first_slot = jnp.arange(slots, dtype=jnp.int32) == 0
    allowed = jnp.where(first_slot[None, :, None], causal[:, None, :], link_on[None, :, None])
    scores = (
        jnp.einsum("sthc,msuhc->shtmu", query_heads, key_near, preferred_element_type=jnp.float32)
        * score_scale
    )
    scores = jnp.where(allowed[None, None], scores, -jnp.inf)
    row_max = jnp.max(scores, axis=(3, 4), keepdims=True)
    raw = jnp.exp(scores - row_max)
    softmax = raw / jnp.sum(raw, axis=(3, 4), keepdims=True)
    probs_low = softmax.astype(jnp.bfloat16)
    attended = jnp.einsum(
        "shtmu,msuhc->sthc", probs_low, value_near, preferred_element_type=jnp.float32
    ).astype(jnp.bfloat16)
    grad_rows = grad_out.reshape(local_seqs * block_len, D)
    w_rows = w_out.shape[0]
    inputs_out = jnp.concatenate([grad_rows.reshape(-1, w_out.shape[1]), w_out], axis=0)
    inputs_in = swapped(inputs_out, "fsdp", 0)
    grad_rows_other = inputs_in[:-w_rows].reshape(grad_rows.shape)
    w_other = inputs_in[-w_rows:]
    columns = grad_rows
    w_first = lax.axis_index("fsdp") == 0
    w_full = jnp.where(
        w_first, jnp.concatenate([w_out, w_other], axis=1), jnp.concatenate([w_other, w_out], axis=1)
    )
    grad_att = lax.dot_general(
        columns,
        w_full,
        (((1,), (1,)), ((), ())),
        preferred_element_type=jnp.float32,
    ).astype(jnp.bfloat16)
    grad_heads = grad_att.reshape(local_seqs, block_len, local_heads, HD)
    attended_rows = attended.reshape(local_seqs * block_len, local_width)
    fsdp_size = lax.axis_size("fsdp")
    fsdp_at = lax.axis_index("fsdp")
    share = local_width // fsdp_size
    own_cols = lax.dynamic_slice_in_dim(attended_rows, fsdp_at * share, share, axis=1)
    given_cols = lax.dynamic_slice_in_dim(attended_rows, (1 - fsdp_at) * share, share, axis=1)
    taken_cols = swapped(given_cols, "fsdp", 0)
    token_rows = jnp.concatenate([grad_rows, grad_rows_other], axis=0)
    token_cols = jnp.concatenate([own_cols, taken_cols], axis=0)
    partial = lax.dot_general(
        token_rows, token_cols, (((0,), (0,)), ((), ())), preferred_element_type=jnp.float32
    )
    n_hi = lax.axis_size("seq_hi")
    n_lo = lax.axis_size("seq_lo")
    pieces = partial.reshape(n_hi, n_lo, partial.shape[0] // (n_hi * n_lo), partial.shape[1])
    inner = lax.all_to_all(pieces.astype(jnp.bfloat16), "seq_lo", 1, 1, tiled=False)
    inner = jnp.sum(inner.astype(jnp.float32), axis=1)
    outer = lax.all_to_all(inner.astype(jnp.bfloat16), "seq_hi", 0, 0, tiled=False)
    grad_w = jnp.sum(outer.astype(jnp.float32), axis=0)
    grad_probs = jnp.einsum(
        "sthc,msuhc->shtmu", grad_heads, value_near, preferred_element_type=jnp.float32
    )
    row_dot = jnp.sum(softmax * grad_probs, axis=(3, 4), keepdims=True)
    grad_scores = (softmax * (grad_probs - row_dot) * score_scale).astype(jnp.bfloat16)
    grad_query = jnp.einsum(
        "shtmu,msuhc->sthc", grad_scores, key_near, preferred_element_type=jnp.float32
    ).astype(jnp.bfloat16)
    key_terms = jnp.einsum(
        "shtmu,sthc->msuhc", grad_scores, query_heads, preferred_element_type=jnp.float32
    )
    value_terms = jnp.einsum(
        "shtmu,sthc->msuhc", probs_low, grad_heads, preferred_element_type=jnp.float32
    )
    grad_key = key_terms[0]
    grad_value = value_terms[0]
    for level in range(levels):
        outgoing = jnp.stack([key_terms[level + 1], value_terms[level + 1]]).astype(jnp.bfloat16)
        returned = swapped(outgoing, SEQ, level)
        grad_key = grad_key + returned[0].astype(jnp.float32)
        grad_value = grad_value + returned[1].astype(jnp.float32)
    shape_out = (local_seqs, block_len, local_width)
    return (
        grad_query.reshape(shape_out),
        grad_key.astype(jnp.bfloat16).reshape(shape_out),
        grad_value.astype(jnp.bfloat16).reshape(shape_out),
        grad_w,
    )


def solution(mesh):
    n_seq = mesh.shape["seq"]
    n_lo = min(8, n_seq)
    devices = mesh.devices.reshape(n_seq // n_lo, n_lo, *mesh.devices.shape[1:])
    mesh = jax.sharding.Mesh(devices, SEQ + mesh.axis_names[1:])
    in_specs = (
        P("fsdp", SEQ, "head"),
        P("fsdp", SEQ, "head"),
        P("fsdp", SEQ, "head"),
        P("fsdp", SEQ, None),
        P("head", "fsdp"),
        P(SEQ, None),
    )
    out_specs = (
        P("fsdp", SEQ, "head"),
        P("fsdp", SEQ, "head"),
        P("fsdp", SEQ, "head"),
        P(SEQ, ("head", "fsdp")),
    )
    return jax.shard_map(
        per_device_body, mesh=mesh, in_specs=in_specs, out_specs=out_specs, check_vma=False
    )
```

```python
import math

import jax
import jax.numpy as jnp
from jax import lax
from jax.sharding import PartitionSpec as P


D = 4096
HD = 128


SEQ = ("seq_hi", "seq_lo")


def size_of(axis):
    names = axis if isinstance(axis, tuple) else (axis,)
    return math.prod(lax.axis_size(name) for name in names)


def swapped(shard, axis, distance):
    return lax.ppermute(shard, axis, [(i, i ^ 1 << distance) for i in range(size_of(axis))])


def per_device_body(query, keys, values, grad_out, w_out, link_flags):
    local_seqs, block_len, local_width = query.shape
    local_heads = local_width // HD
    levels = size_of(SEQ).bit_length() - 1
    score_scale = 1.0 / math.sqrt(HD)
    key_value = jnp.stack([keys, values])
    collected = [key_value]
    for level in range(levels):
        collected.append(swapped(key_value, SEQ, level))
    slots = levels + 1
    near_all = jnp.stack(collected).reshape(slots, 2, local_seqs, block_len, local_heads, HD)
    key_near = near_all[:, 0]
    value_near = near_all[:, 1]
    query_heads = query.reshape(local_seqs, block_len, local_heads, HD)
    spots = jnp.arange(block_len, dtype=jnp.int32)
    causal = spots[None, :] <= spots[:, None]
    link_on = jnp.concatenate([jnp.ones((1,), dtype=bool), link_flags[0] > 0])
    first_slot = jnp.arange(slots, dtype=jnp.int32) == 0
    allowed = jnp.where(first_slot[None, :, None], causal[:, None, :], link_on[None, :, None])
    scores = (
        jnp.einsum("sthc,msuhc->shtmu", query_heads, key_near, preferred_element_type=jnp.float32)
        * score_scale
    )
    scores = jnp.where(allowed[None, None], scores, -jnp.inf)
    row_max = jnp.max(scores, axis=(3, 4), keepdims=True)
    raw = jnp.exp(scores - row_max)
    softmax = raw / jnp.sum(raw, axis=(3, 4), keepdims=True)
    probs_low = softmax.astype(jnp.bfloat16)
    attended = jnp.einsum(
        "shtmu,msuhc->sthc", probs_low, value_near, preferred_element_type=jnp.float32
    ).astype(jnp.bfloat16)
    grad_rows = grad_out.reshape(local_seqs * block_len, D)
    grad_rows_other = swapped(grad_rows, "fsdp", 0)
    columns = grad_rows
    w_other = swapped(w_out, "fsdp", 0)
    w_first = lax.axis_index("fsdp") == 0
    w_full = jnp.where(
        w_first, jnp.concatenate([w_out, w_other], axis=1), jnp.concatenate([w_other, w_out], axis=1)
    )
    grad_att = lax.dot_general(
        columns,
        w_full,
        (((1,), (1,)), ((), ())),
        preferred_element_type=jnp.float32,
    ).astype(jnp.bfloat16)
    grad_heads = grad_att.reshape(local_seqs, block_len, local_heads, HD)
    attended_rows = attended.reshape(local_seqs * block_len, local_width)
    fsdp_size = lax.axis_size("fsdp")
    fsdp_at = lax.axis_index("fsdp")
    share = local_width // fsdp_size
    own_cols = lax.dynamic_slice_in_dim(attended_rows, fsdp_at * share, share, axis=1)
    given_cols = lax.dynamic_slice_in_dim(attended_rows, (1 - fsdp_at) * share, share, axis=1)
    taken_cols = swapped(given_cols, "fsdp", 0)
    token_rows = jnp.concatenate([grad_rows, grad_rows_other], axis=0)
    token_cols = jnp.concatenate([own_cols, taken_cols], axis=0)
    partial = lax.dot_general(
        token_rows, token_cols, (((0,), (0,)), ((), ())), preferred_element_type=jnp.float32
    )
    n_hi = lax.axis_size("seq_hi")
    n_lo = lax.axis_size("seq_lo")
    pieces = partial.reshape(n_hi, n_lo, partial.shape[0] // (n_hi * n_lo), partial.shape[1])
    inner = lax.all_to_all(pieces.astype(jnp.bfloat16), "seq_lo", 1, 1, tiled=False)
    inner = jnp.sum(inner.astype(jnp.float32), axis=1)
    outer = lax.all_to_all(inner.astype(jnp.bfloat16), "seq_hi", 0, 0, tiled=False)
    grad_w = jnp.sum(outer.astype(jnp.float32), axis=0)
    grad_probs = jnp.einsum(
        "sthc,msuhc->shtmu", grad_heads, value_near, preferred_element_type=jnp.float32
    )
    row_dot = jnp.sum(softmax * grad_probs, axis=(3, 4), keepdims=True)
    grad_scores = (softmax * (grad_probs - row_dot) * score_scale).astype(jnp.bfloat16)
    grad_query = jnp.einsum(
        "shtmu,msuhc->sthc", grad_scores, key_near, preferred_element_type=jnp.float32
    ).astype(jnp.bfloat16)
    key_terms = jnp.einsum(
        "shtmu,sthc->msuhc", grad_scores, query_heads, preferred_element_type=jnp.float32
    )
    value_terms = jnp.einsum(
        "shtmu,sthc->msuhc", probs_low, grad_heads, preferred_element_type=jnp.float32
    )
    grad_key = key_terms[0]
    grad_value = value_terms[0]
    for level in range(levels):
        outgoing = jnp.stack([key_terms[level + 1], value_terms[level + 1]]).astype(jnp.bfloat16)
        returned = swapped(outgoing, SEQ, level)
        grad_key = grad_key + returned[0].astype(jnp.float32)
        grad_value = grad_value + returned[1].astype(jnp.float32)
    shape_out = (local_seqs, block_len, local_width)
    return (
        grad_query.reshape(shape_out),
        grad_key.astype(jnp.bfloat16).reshape(shape_out),
        grad_value.astype(jnp.bfloat16).reshape(shape_out),
        grad_w,
    )


def solution(mesh):
    n_seq = mesh.shape["seq"]
    n_lo = min(8, n_seq)
    devices = mesh.devices.reshape(n_seq // n_lo, n_lo, *mesh.devices.shape[1:])
    mesh = jax.sharding.Mesh(devices, SEQ + mesh.axis_names[1:])
    in_specs = (
        P("fsdp", SEQ, "head"),
        P("fsdp", SEQ, "head"),
        P("fsdp", SEQ, "head"),
        P("fsdp", SEQ, None),
        P("head", "fsdp"),
        P(SEQ, None),
    )
    out_specs = (
        P("fsdp", SEQ, "head"),
        P("fsdp", SEQ, "head"),
        P("fsdp", SEQ, "head"),
        P(SEQ, ("head", "fsdp")),
    )
    return jax.shard_map(
        per_device_body, mesh=mesh, in_specs=in_specs, out_specs=out_specs, check_vma=False
    )
```
